32 devices in a mesh: blk: 4 (over y, core), grp: 8 (over z, x).
Axes of the slice: x: 2, y: 2, z: 4, core: 2. Of those that a mesh axis runs over, the one named last changes fastest.
Arguments:
- features: bfloat16 [4096, 256], P(('blk', 'grp')), may hold values from -6 to 6
- weights: bfloat16 [2, 256, 256], replicated, may hold values from -0.375 to 0.375
- biases: float32 [2, 256], replicated, may hold values from -0.6 to 0.6
- adjacency: bfloat16 [4, 8, 6, 256, 256], P('blk', 'grp'), as said below
- tile_row: int32 [4, 8, 6], P('blk', 'grp'), may hold values from 0 to 1
- tile_column: int32 [4, 8, 6], P('blk', 'grp'), may hold values from 0 to 3
- tile_count: int32 [4, 8], P('blk', 'grp'), may hold values from 1 to 6, as said below
Outputs:
- result: bfloat16 [4096, 256], P(('blk', 'grp'))
The draws below stay inside these ranges and needn't reach their ends.
Inputs may be any that keep to these rules, and one draw needn't show every extreme that they name: tile_count is at least 1 and at most 6; some device has exactly 6 live slots. `adjacency`: edge weights are zero or positive.
All inputs are finite; a program needn't handle non-finite values.
Results may differ from the reference program's by a relative error of at most 0.0046.
Values may be sent and summed in bfloat16 or wider, within the bound.
No kernel may reach another device: no remote copies, remote signals or barrier semaphores. Data moves between devices by JAX's collectives and lax.ppermute only.
A program may use at most 64 MiB of HBM per device.

```python
import math
import jax
import jax.numpy as jnp
from jax import lax

F = 256
TILE = 256
LAYERS = 2
NODE_DEV = 128
TILES = 6
NODES = 4096
ROW_TILES = 2
COL_TILES = 4
N_BLK = 4
N_GRP = 8


def draw_adjacency(key, part):
    first, second = jax.random.split(key, 2)
    shape = (N_BLK, N_GRP, TILES, TILE, TILE)
    uniform_draw = jax.random.uniform(first, shape, jnp.float32)
    density = jnp.exp(math.log(10.0) * jax.random.uniform(second, (N_BLK, N_GRP, TILES, 1, 1), jnp.float32)) / TILE
    weight_value = jnp.ones(shape, jnp.float32)
    values = jnp.where(uniform_draw < density, weight_value, 0.0)
    return values.astype(jnp.bfloat16)


def draw_tile_count(key, part):
    first, second = jax.random.split(jax.random.fold_in(key, 7))
    raw = jax.random.randint(first, (N_BLK * N_GRP,), 0, TILES + 1)
    counts = 1 + raw * raw // (TILES + 1)
    chosen = jax.random.randint(second, (), 0, N_BLK * N_GRP)
    counts = counts.at[chosen].set(TILES)
    return counts.reshape(N_BLK, N_GRP).astype(jnp.int32)


def touch_ends(entries, stream_key, smallest, largest):
    dims = entries.shape
    place = [jax.random.randint(jax.random.fold_in(stream_key, axis), (), 0, dims[axis]) for axis in range(len(dims))]
    entries = entries.at[tuple(place)].set(smallest)
    longest = dims.index(max(dims))
    place[longest] = (place[longest] + 1) % dims[longest]
    return entries.at[tuple(place)].set(largest)


def block_scale(own_key, shape, pieces, low, top_value):
    def one(dim, blocks):
        steps = jax.random.uniform(jax.random.fold_in(jax.random.fold_in(own_key, 6), dim), (blocks,), jnp.float32, low / len(pieces), top_value / len(pieces))
        return jnp.repeat(jnp.exp(steps), shape[dim] // blocks).reshape((-1,) + (1,) * (len(shape) - dim - 1))

    gain = one(*pieces[0])
    for cut in pieces[1:]:
        gain = gain * one(*cut)
    return gain


def centred(own_key, dims, spread, reach, pieces=(), kind=jnp.bfloat16):
    factor_of = block_scale(own_key, dims, pieces, -0.22, 0.18) if pieces else 1.0
    values = jax.random.normal(own_key, dims, jnp.float32) * spread * factor_of
    return jnp.minimum(jnp.maximum(values, -reach), reach).astype(kind)


def setup_inputs(seed: int = 0) -> dict:
    keys = jax.random.split(jax.random.key(seed), 8)
    return {
        "features": centred(keys[0], (NODES, F), 1.0, 6.0, ((0, 32),)),
        "weights": centred(keys[1], (LAYERS, F, F), F ** -0.5, 0.375),
        "biases": centred(keys[2], (LAYERS, F), 0.1, 0.6, (), jnp.float32),
        "adjacency": draw_adjacency(jax.random.fold_in(keys[7], 71), 0),
        "tile_row": touch_ends(jax.random.randint(keys[4], (N_BLK, N_GRP, TILES), 0, ROW_TILES), jax.random.fold_in(keys[4], 1), 0, ROW_TILES - 1).astype(jnp.int32),
        "tile_column": touch_ends(jax.random.randint(keys[5], (N_BLK, N_GRP, TILES), 0, COL_TILES), jax.random.fold_in(keys[5], 1), 0, COL_TILES - 1).astype(jnp.int32),
        "tile_count": draw_tile_count(jax.random.fold_in(keys[7], 71), 0),
    }


def reference(features, weights, biases, adjacency, tile_row, tile_column, tile_count):
    devices_all = N_BLK * N_GRP
    row_tiles = N_BLK * NODE_DEV // TILE
    col_tiles = N_GRP * NODE_DEV // TILE
    flat_tiles = adjacency.reshape(devices_all, TILES, TILE, TILE)
    flat_rows = tile_row.reshape(devices_all, TILES).astype(jnp.int32)
    flat_cols = tile_column.reshape(devices_all, TILES).astype(jnp.int32)
    slot_ids = jnp.arange(TILES, dtype=jnp.int32)
    live = (slot_ids[None, :] < tile_count.reshape(devices_all, 1)).astype(jnp.float32)
    device_ids = jnp.arange(devices_all, dtype=jnp.int32)

    def to_owners(parts):
        shaped = parts.reshape((N_BLK, N_GRP, N_BLK, NODE_DEV) + parts.shape[2:])
        summed = lax.optimization_barrier(jnp.sum(shaped, axis=0))
        order = (1, 0) + tuple(range(2, summed.ndim))
        return jnp.transpose(summed, order).reshape((NODES,) + parts.shape[2:])

    def degree_part(inputs):
        tiles_one, rows_one, live_one = inputs
        sums = lax.optimization_barrier(jnp.sum(tiles_one.astype(jnp.float32), axis=2)) * live_one[:, None]
        return jnp.zeros((row_tiles, TILE), jnp.float32).at[rows_one].add(sums).reshape(row_tiles * TILE)
    degree = 1.0 + to_owners(lax.map(degree_part, (flat_tiles, flat_rows, live)))
    scale = lax.rsqrt(degree)[:, None]
    hidden = features
    result = None
    for layer_index in range(LAYERS):
        mixed = jnp.dot(hidden, weights[layer_index], preferred_element_type=jnp.float32)
        scaled = (mixed * scale).astype(jnp.bfloat16)
        groups = scaled.reshape(N_BLK, N_GRP * NODE_DEV, F)

        def device_part(inputs):
            index, tiles_one, rows_one, cols_one, live_one = inputs
            column_group = index // N_GRP
            columns = lax.dynamic_slice_in_dim(groups, column_group, 1, 0)[0]
            blocks = columns.reshape(col_tiles, TILE, F)[cols_one]
            prod = jnp.einsum('tij,tjf->tif', tiles_one.astype(jnp.float32), blocks.astype(jnp.float32))
            prod = prod * live_one[:, None, None]
            total = jnp.zeros((row_tiles, TILE, F), jnp.float32).at[rows_one].add(prod)
            return total.reshape(row_tiles * TILE, F)
        gathered = to_owners(lax.map(device_part, (device_ids, flat_tiles, flat_rows, flat_cols, live)))
        pre = (gathered + scaled.astype(jnp.float32)) * scale + biases[layer_index][None, :]
        if layer_index < LAYERS - 1:
            hidden = jnp.maximum(pre, 0.0).astype(jnp.bfloat16)
        else:
            result = pre.astype(jnp.bfloat16)
    return result
```

```python
import jax
import jax.numpy as jnp
from jax import lax
from jax.sharding import PartitionSpec as P

LAYERS = 2


def gather_group(block, axis, size):
    received = [block]
    for shift in range(1, size):
        perm = [(i, (i - shift) % size) for i in range(size)]
        received.append(lax.ppermute(block, axis, perm=perm))
    return jnp.stack(received)


def scatter_sum(parts, axis, size):
    me = lax.axis_index(axis)
    total = lax.dynamic_index_in_dim(parts, me, 0, keepdims=False)
    for shift in range(1, size):
        perm = [(i, (i + shift) % size) for i in range(size)]
        outgoing = lax.dynamic_index_in_dim(parts, (me + shift) % size, 0, keepdims=False)
        total = total + lax.ppermute(outgoing, axis, perm=perm)
    return total


def on_device(features, weights, biases, adjacency, tile_row, tile_column, tile_count):
    adjacency = adjacency[0, 0]
    rows_here = tile_row[0, 0]
    cols_here = tile_column[0, 0]
    count_here = tile_count[0, 0]
    blk_size = lax.axis_size("blk")
    grp_size = lax.axis_size("grp")
    node_dev = features.shape[0]
    tile_size = adjacency.shape[1]
    slots = adjacency.shape[0]
    width = features.shape[1]
    row_tiles = blk_size * node_dev // tile_size
    per_tile = tile_size // node_dev
    live = lax.iota(jnp.int32, slots) < count_here
    placing = (
        (rows_here[None, :] == lax.iota(jnp.int32, row_tiles)[:, None]) & live[None, :]
    ).astype(jnp.float32)
    row_sums = jnp.sum(adjacency, axis=2, dtype=jnp.float32)
    degree_part = jnp.dot(placing, row_sums, precision=lax.Precision.HIGHEST).reshape(
        blk_size, node_dev
    )
    degree = scatter_sum(degree_part, "blk", blk_size)
    scale = lax.rsqrt(1.0 + degree)[:, None]
    me_grp = lax.axis_index("grp")
    sources = cols_here[:, None] * per_tile + lax.iota(jnp.int32, per_tile)[None, :]
    slot_of_source = (sources - me_grp) % grp_size
    hidden = features
    result = None
    for layer_index in range(LAYERS):
        mixed = jnp.dot(hidden, weights[layer_index], preferred_element_type=jnp.float32)
        scaled = (mixed * scale).astype(jnp.bfloat16)
        received = gather_group(scaled, "grp", grp_size)
        blocks = received[slot_of_source].reshape(slots, tile_size, width)
        product = jnp.einsum("tij,tjf->tif", adjacency, blocks, preferred_element_type=jnp.float32)
        placed = jnp.einsum("rt,tif->rif", placing, product, precision=lax.Precision.HIGHEST)
        partial_value = placed.reshape(blk_size, node_dev, width)
        summed = scatter_sum(partial_value, "blk", blk_size)
        pre = (summed + scaled.astype(jnp.float32)) * scale + biases[layer_index][None, :]
        if layer_index < LAYERS - 1:
            hidden = jnp.maximum(pre, 0.0).astype(jnp.bfloat16)
        else:
            result = pre.astype(jnp.bfloat16)
    return result


def solution(mesh):
    placed = (
        P(("blk", "grp"), None),
        P(),
        P(),
        P("blk", "grp", None, None, None),
        P("blk", "grp", None),
        P("blk", "grp", None),
        P("blk", "grp"),
    )
    return jax.shard_map(
        on_device, mesh=mesh, in_specs=placed, out_specs=P(("blk", "grp"), None), check_vma=False
    )
```

```python
import jax
import jax.numpy as jnp
from jax import lax
from jax.sharding import PartitionSpec as P

LAYERS = 2


def gather_group(block, axis, size):
    received = [block]
    for shift in range(1, size):
        perm = [(i, (i - shift) % size) for i in range(size)]
        received.append(lax.ppermute(block, axis, perm=perm))
    return jnp.stack(received)


def scatter_sum(parts, axis, size):
    me = lax.axis_index(axis)
    total = lax.dynamic_index_in_dim(parts, me, 0, keepdims=False)
    for shift in range(1, size):
        perm = [(i, (i + shift) % size) for i in range(size)]
        outgoing = lax.dynamic_index_in_dim(parts, (me + shift) % size, 0, keepdims=False)
        total = total + lax.ppermute(outgoing, axis, perm=perm)
    return total


def on_device(features, weights, biases, adjacency, tile_row, tile_column, tile_count):
    adjacency = adjacency[0, 0]
    rows_here = tile_row[0, 0]
    cols_here = tile_column[0, 0]
    count_here = tile_count[0, 0]
    blk_size = lax.axis_size("blk")
    grp_size = lax.axis_size("grp")
    node_dev = features.shape[0]
    tile_size = adjacency.shape[1]
    slots = adjacency.shape[0]
    width = features.shape[1]
    row_tiles = blk_size * node_dev // tile_size
    per_tile = tile_size // node_dev

    group_features = gather_group(features, "grp", grp_size)

    live = lax.iota(jnp.int32, slots) < count_here
    placing = (rows_here[None, :] == lax.iota(jnp.int32, row_tiles)[:, None]) & live[None, :]
    masked = jnp.where(placing[:, :, None, None], adjacency[None], jnp.zeros((), adjacency.dtype))
    lhs = masked.transpose(0, 2, 1, 3).reshape(row_tiles * tile_size, slots * tile_size)
    ones = jnp.ones((slots * tile_size, 128), adjacency.dtype)
    row_sums = jnp.dot(lhs, ones, preferred_element_type=jnp.float32)[:, 0]
    degree = scatter_sum(row_sums.reshape(blk_size, node_dev), "blk", blk_size)
    norm = lax.rsqrt(1.0 + degree)
    group_norm = gather_group(norm, "grp", grp_size)

    me_grp = lax.axis_index("grp")
    sources = cols_here[:, None] * per_tile + lax.iota(jnp.int32, per_tile)[None, :]
    slot_of_source = (sources - me_grp) % grp_size
    scale = norm[:, None]
    hidden = features
    result = None
    for layer_index in range(LAYERS):
        if layer_index == 0:
            mixed = jnp.dot(
                group_features.reshape(grp_size * node_dev, width),
                weights[layer_index],
                preferred_element_type=jnp.float32,
            ).reshape(grp_size, node_dev, width)
            received = (mixed * group_norm[:, :, None]).astype(jnp.bfloat16)
            scaled = received[0]
        else:
            mixed = jnp.dot(hidden, weights[layer_index], preferred_element_type=jnp.float32)
            scaled = (mixed * scale).astype(jnp.bfloat16)
            received = gather_group(scaled, "grp", grp_size)
        rhs = received[slot_of_source].reshape(slots * tile_size, width)
        placed = jnp.dot(lhs, rhs, preferred_element_type=jnp.float32)
        partial_value = placed.reshape(blk_size, node_dev, width)
        summed = scatter_sum(partial_value, "blk", blk_size)
        pre = (summed + scaled.astype(jnp.float32)) * scale + biases[layer_index][None, :]
        if layer_index < LAYERS - 1:
            hidden = jnp.maximum(pre, 0.0).astype(jnp.bfloat16)
        else:
            result = pre.astype(jnp.bfloat16)
    return result


def solution(mesh):
    placed = (
        P(("blk", "grp"), None),
        P(),
        P(),
        P("blk", "grp", None, None, None),
        P("blk", "grp", None),
        P("blk", "grp", None),
        P("blk", "grp"),
    )
    return jax.shard_map(
        on_device, mesh=mesh, in_specs=placed, out_specs=P(("blk", "grp"), None), check_vma=False
    )
```

```python
import jax
import jax.numpy as jnp
from jax import lax
from jax.sharding import PartitionSpec as P

LAYERS = 2
TWO_STAGE_GATHER = False


def gather_group(block, axis, size):
    received = [block]
    for shift in range(1, size):
        perm = [(i, (i - shift) % size) for i in range(size)]
        received.append(lax.ppermute(block, axis, perm=perm))
    return jnp.stack(received)


def gather_tiles(block, axis, size, per_tile):
    me = lax.axis_index(axis)
    pos = me % per_tile
    parts = [block]
    for shift in range(1, per_tile):
        perm = [(i, i - i % per_tile + (i + shift) % per_tile) for i in range(size)]
        parts.append(lax.ppermute(block, axis, perm=perm))
    stacked = jnp.stack(parts)
    order = (lax.iota(jnp.int32, per_tile) - pos) % per_tile
    tile = stacked[order]
    tiles = [tile]
    n_tiles = size // per_tile
    for shift in range(1, n_tiles):
        perm = [(i, (i - shift * per_tile) % size) for i in range(size)]
        tiles.append(lax.ppermute(tile, axis, perm=perm))
    return jnp.stack(tiles)


def scatter_sum(parts, axis, size):
    me = lax.axis_index(axis)
    total = lax.dynamic_index_in_dim(parts, me, 0, keepdims=False)
    for shift in range(1, size):
        perm = [(i, (i + shift) % size) for i in range(size)]
        outgoing = lax.dynamic_index_in_dim(parts, (me + shift) % size, 0, keepdims=False)
        total = total + lax.ppermute(outgoing, axis, perm=perm)
    return total


def scatter_sum_pairs(parts, axis, size):
    if size % 2:
        return scatter_sum(parts, axis, size)
    me = lax.axis_index(axis)
    low = me % 2
    by_pair = parts.reshape((size // 2, 2) + parts.shape[1:])
    mine = lax.dynamic_index_in_dim(by_pair, low, 1, keepdims=False)
    theirs = lax.dynamic_index_in_dim(by_pair, 1 - low, 1, keepdims=False)
    perm = [(i, i ^ 1) for i in range(size)]
    half = mine + lax.ppermute(theirs, axis, perm=perm)
    pair_me = me // 2
    total = lax.dynamic_index_in_dim(half, pair_me, 0, keepdims=False)
    for shift in range(1, size // 2):
        perm = [(i, (i + 2 * shift) % size) for i in range(size)]
        outgoing = lax.dynamic_index_in_dim(half, (pair_me + shift) % (size // 2), 0, keepdims=False)
        total = total + lax.ppermute(outgoing, axis, perm=perm)
    return total


def on_device(features, weights, biases, adjacency, tile_row, tile_column, tile_count):
    adjacency = adjacency[0, 0]
    rows_here = tile_row[0, 0]
    cols_here = tile_column[0, 0]
    count_here = tile_count[0, 0]
    blk_size = lax.axis_size("blk")
    grp_size = lax.axis_size("grp")
    node_dev = features.shape[0]
    tile_size = adjacency.shape[1]
    slots = adjacency.shape[0]
    width = features.shape[1]
    row_tiles = blk_size * node_dev // tile_size
    per_tile = tile_size // node_dev
    live = lax.iota(jnp.int32, slots) < count_here
    placing = (rows_here[:, None] == lax.iota(jnp.int32, row_tiles)[None, :]) & live[:, None]
    lhs = adjacency.transpose(1, 0, 2).reshape(tile_size, slots * tile_size)
    pick = jnp.broadcast_to(placing[:, None, :, None], (slots, tile_size, row_tiles, 128))
    row_sums = jnp.dot(
        lhs, pick.astype(adjacency.dtype).reshape(slots * tile_size, row_tiles * 128),
        preferred_element_type=jnp.float32,
    )
    degree_part = row_sums.reshape(tile_size, row_tiles, 128)[:, :, 0].T.reshape(blk_size, node_dev)
    degree = scatter_sum_pairs(degree_part, "blk", blk_size)
    scale = lax.rsqrt(1.0 + degree)[:, None]
    me_grp = lax.axis_index("grp")
    hidden = features
    result = None
    for layer_index in range(LAYERS):
        mixed = jnp.dot(hidden, weights[layer_index], preferred_element_type=jnp.float32)
        scaled = (mixed * scale).astype(jnp.bfloat16)
        if TWO_STAGE_GATHER and per_tile > 1 and grp_size % per_tile == 0:
            tiles = gather_tiles(scaled, "grp", grp_size, per_tile)
            n_tiles = grp_size // per_tile
            blocks = tiles[(cols_here - me_grp // per_tile) % n_tiles].reshape(slots, tile_size, width)
        else:
            received = gather_group(scaled, "grp", grp_size)
            sources = cols_here[:, None] * per_tile + lax.iota(jnp.int32, per_tile)[None, :]
            blocks = received[(sources - me_grp) % grp_size].reshape(slots, tile_size, width)
        rhs = jnp.where(
            placing[:, None, :, None], blocks[:, :, None, :], jnp.zeros((), blocks.dtype)
        ).reshape(slots * tile_size, row_tiles * width)
        out = jnp.dot(lhs, rhs, preferred_element_type=jnp.float32)
        partial_value = (
            out.reshape(per_tile, node_dev, row_tiles, width).transpose(2, 0, 1, 3)
            .reshape(blk_size, node_dev, width)
        )
        summed = scatter_sum_pairs(partial_value, "blk", blk_size)
        pre = (summed + scaled.astype(jnp.float32)) * scale + biases[layer_index][None, :]
        if layer_index < LAYERS - 1:
            hidden = jnp.maximum(pre, 0.0).astype(jnp.bfloat16)
        else:
            result = pre.astype(jnp.bfloat16)
    return result


def solution(mesh):
    placed = (
        P(("blk", "grp"), None),
        P(),
        P(),
        P("blk", "grp", None, None, None),
        P("blk", "grp", None),
        P("blk", "grp", None),
        P("blk", "grp"),
    )
    return jax.shard_map(
        on_device, mesh=mesh, in_specs=placed, out_specs=P(("blk", "grp"), None), check_vma=False
    )
```

```python
import jax
import jax.numpy as jnp
from jax import lax
from jax.sharding import PartitionSpec as P

LAYERS = 2
TWO_STAGE_GATHER = True
SPLIT = True


def gather_group(block, axis, size):
    received = [block]
    for shift in range(1, size):
        perm = [(i, (i - shift) % size) for i in range(size)]
        received.append(lax.ppermute(block, axis, perm=perm))
    return jnp.stack(received)


def gather_tiles(block, axis, size, per_tile):
    me = lax.axis_index(axis)
    pos = me % per_tile
    parts = [block]
    for shift in range(1, per_tile):
        perm = [(i, i - i % per_tile + (i + shift) % per_tile) for i in range(size)]
        parts.append(lax.ppermute(block, axis, perm=perm))
    stacked = jnp.stack(parts)
    order = (lax.iota(jnp.int32, per_tile) - pos) % per_tile
    tile = stacked[order]
    tiles = [tile]
    n_tiles = size // per_tile
    for shift in range(1, n_tiles):
        perm = [(i, (i - shift * per_tile) % size) for i in range(size)]
        tiles.append(lax.ppermute(tile, axis, perm=perm))
    return jnp.stack(tiles)


def gather_outer_first(block, axis, size, per_tile, split):
    me = lax.axis_index(axis)
    pos = me % per_tile
    n_tiles = size // per_tile
    outer = [block]
    for shift in range(1, n_tiles):
        perm = [(i, (i - shift * per_tile) % size) for i in range(size)]
        outer.append(lax.ppermute(block, axis, perm=perm))
    full = [jnp.stack(outer)]
    for shift in range(1, per_tile):
        perm = [(i, i - i % per_tile + (i - shift) % per_tile) for i in range(size)]
        if split:
            full.append(jnp.stack([lax.ppermute(part, axis, perm=perm) for part in outer]))
        else:
            full.append(lax.ppermute(full[0], axis, perm=perm))
    stacked = jnp.stack(full)
    order = (lax.iota(jnp.int32, per_tile) - pos) % per_tile
    return jnp.swapaxes(stacked[order], 0, 1)


def scatter_sum(parts, axis, size):
    me = lax.axis_index(axis)
    total = lax.dynamic_index_in_dim(parts, me, 0, keepdims=False)
    for shift in range(1, size):
        perm = [(i, (i + shift) % size) for i in range(size)]
        outgoing = lax.dynamic_index_in_dim(parts, (me + shift) % size, 0, keepdims=False)
        total = total + lax.ppermute(outgoing, axis, perm=perm)
    return total


def scatter_sum_pairs(parts, axis, size):
    if size % 2:
        return scatter_sum(parts, axis, size)
    me = lax.axis_index(axis)
    low = me % 2
    by_pair = parts.reshape((size // 2, 2) + parts.shape[1:])
    mine = lax.dynamic_index_in_dim(by_pair, low, 1, keepdims=False)
    theirs = lax.dynamic_index_in_dim(by_pair, 1 - low, 1, keepdims=False)
    perm = [(i, i ^ 1) for i in range(size)]
    half = mine + lax.ppermute(theirs, axis, perm=perm)
    pair_me = me // 2
    total = lax.dynamic_index_in_dim(half, pair_me, 0, keepdims=False)
    for shift in range(1, size // 2):
        perm = [(i, (i + 2 * shift) % size) for i in range(size)]
        outgoing = lax.dynamic_index_in_dim(half, (pair_me + shift) % (size // 2), 0, keepdims=False)
        total = total + lax.ppermute(outgoing, axis, perm=perm)
    return total


def on_device(features, weights, biases, adjacency, tile_row, tile_column, tile_count):
    adjacency = adjacency[0, 0]
    rows_here = tile_row[0, 0]
    cols_here = tile_column[0, 0]
    count_here = tile_count[0, 0]
    blk_size = lax.axis_size("blk")
    grp_size = lax.axis_size("grp")
    node_dev = features.shape[0]
    tile_size = adjacency.shape[1]
    slots = adjacency.shape[0]
    width = features.shape[1]
    row_tiles = blk_size * node_dev // tile_size
    per_tile = tile_size // node_dev
    live = lax.iota(jnp.int32, slots) < count_here
    placing = (rows_here[:, None] == lax.iota(jnp.int32, row_tiles)[None, :]) & live[:, None]
    lhs = adjacency.transpose(1, 0, 2).reshape(tile_size, slots * tile_size)
    slot_mask = jnp.broadcast_to(placing.T[:, None, :, None], (row_tiles, 1, slots, tile_size))
    placed_lhs = jnp.where(
        slot_mask.reshape(row_tiles, 1, slots * tile_size), lhs[None], jnp.zeros((), lhs.dtype)
    ).reshape(row_tiles * tile_size, slots * tile_size)
    pick = jnp.broadcast_to(placing[:, None, :, None], (slots, tile_size, row_tiles, 128))
    row_sums = jnp.dot(
        lhs, pick.astype(adjacency.dtype).reshape(slots * tile_size, row_tiles * 128),
        preferred_element_type=jnp.float32,
    )
    degree_part = row_sums.reshape(tile_size, row_tiles, 128)[:, :, 0].T.reshape(blk_size, node_dev)
    degree = scatter_sum_pairs(degree_part, "blk", blk_size)
    scale = lax.rsqrt(1.0 + degree)[:, None]
    me_grp = lax.axis_index("grp")
    hidden = features
    result = None
    for layer_index in range(LAYERS):
        mixed = jnp.dot(hidden, weights[layer_index], preferred_element_type=jnp.float32)
        scaled = (mixed * scale).astype(jnp.bfloat16)
        if TWO_STAGE_GATHER and per_tile > 1 and grp_size % per_tile == 0:
            tiles = gather_outer_first(scaled, "grp", grp_size, per_tile, SPLIT)
            n_tiles = grp_size // per_tile
            blocks = tiles[(cols_here - me_grp // per_tile) % n_tiles].reshape(slots, tile_size, width)
        else:
            received = gather_group(scaled, "grp", grp_size)
            sources = cols_here[:, None] * per_tile + lax.iota(jnp.int32, per_tile)[None, :]
            blocks = received[(sources - me_grp) % grp_size].reshape(slots, tile_size, width)
        out = jnp.dot(
            placed_lhs, blocks.reshape(slots * tile_size, width), preferred_element_type=jnp.float32
        )
        partial_value = out.reshape(blk_size, node_dev, width)
        summed = scatter_sum_pairs(partial_value, "blk", blk_size)
        pre = (summed + scaled.astype(jnp.float32)) * scale + biases[layer_index][None, :]
        if layer_index < LAYERS - 1:
            hidden = jnp.maximum(pre, 0.0).astype(jnp.bfloat16)
        else:
            result = pre.astype(jnp.bfloat16)
    return result


def solution(mesh):
    placed = (
        P(("blk", "grp"), None),
        P(),
        P(),
        P("blk", "grp", None, None, None),
        P("blk", "grp", None),
        P("blk", "grp", None),
        P("blk", "grp"),
    )
    return jax.shard_map(
        on_device, mesh=mesh, in_specs=placed, out_specs=P(("blk", "grp"), None), check_vma=False
    )
```

```python
import jax
import jax.numpy as jnp
from jax import lax
from jax.sharding import PartitionSpec as P

LAYERS = 2
TWO_STAGE_GATHER = True
SPLIT = True


def gather_group(block, axis, size):
    received = [block]
    for shift in range(1, size):
        perm = [(i, (i - shift) % size) for i in range(size)]
        received.append(lax.ppermute(block, axis, perm=perm))
    return jnp.stack(received)


def gather_tiles(block, axis, size, per_tile):
    me = lax.axis_index(axis)
    pos = me % per_tile
    parts = [block]
    for shift in range(1, per_tile):
        perm = [(i, i - i % per_tile + (i + shift) % per_tile) for i in range(size)]
        parts.append(lax.ppermute(block, axis, perm=perm))
    stacked = jnp.stack(parts)
    order = (lax.iota(jnp.int32, per_tile) - pos) % per_tile
    tile = stacked[order]
    tiles = [tile]
    n_tiles = size // per_tile
    for shift in range(1, n_tiles):
        perm = [(i, (i - shift * per_tile) % size) for i in range(size)]
        tiles.append(lax.ppermute(tile, axis, perm=perm))
    return jnp.stack(tiles)


def gather_outer_first(block, axis, size, per_tile, split):
    me = lax.axis_index(axis)
    pos = me % per_tile
    n_tiles = size // per_tile
    outer = [block]
    for shift in range(1, n_tiles):
        perm = [(i, (i - shift * per_tile) % size) for i in range(size)]
        outer.append(lax.ppermute(block, axis, perm=perm))
    full = [jnp.stack(outer)]
    for shift in range(1, per_tile):
        perm = [(i, i - i % per_tile + (i - shift) % per_tile) for i in range(size)]
        if split:
            full.append(jnp.stack([lax.ppermute(part, axis, perm=perm) for part in outer]))
        else:
            full.append(lax.ppermute(full[0], axis, perm=perm))
    return jnp.stack(full)


def scatter_sum(parts, axis, size):
    me = lax.axis_index(axis)
    total = lax.dynamic_index_in_dim(parts, me, 0, keepdims=False)
    for shift in range(1, size):
        perm = [(i, (i + shift) % size) for i in range(size)]
        outgoing = lax.dynamic_index_in_dim(parts, (me + shift) % size, 0, keepdims=False)
        total = total + lax.ppermute(outgoing, axis, perm=perm)
    return total


def scatter_sum_pairs(parts, axis, size):
    if size % 2 or size == 2:
        return scatter_sum(parts, axis, size)
    me = lax.axis_index(axis)
    low = me % 2
    pairs = size // 2
    pair_me = me // 2
    by_pair = parts.reshape((pairs, 2) + parts.shape[1:])
    mine = lax.dynamic_index_in_dim(by_pair, low, 1, keepdims=False)
    theirs = lax.dynamic_index_in_dim(by_pair, 1 - low, 1, keepdims=False)
    swap = [(i, i ^ 1) for i in range(size)]
    far = (pair_me + lax.iota(jnp.int32, pairs - 1) + 1) % pairs
    far_sum = mine[far] + lax.ppermute(theirs[far], axis, perm=swap)
    near = lax.dynamic_index_in_dim(theirs, pair_me, 0, keepdims=False)
    total = lax.dynamic_index_in_dim(mine, pair_me, 0, keepdims=False)
    for shift in range(1, pairs):
        perm = [(i, (i + 2 * shift) % size) for i in range(size)]
        total = total + lax.ppermute(far_sum[shift - 1], axis, perm=perm)
    return total + lax.ppermute(near, axis, perm=swap)


def on_device(features, weights, biases, adjacency, tile_row, tile_column, tile_count):
    adjacency = adjacency[0, 0]
    rows_here = tile_row[0, 0]
    cols_here = tile_column[0, 0]
    count_here = tile_count[0, 0]
    blk_size = lax.axis_size("blk")
    grp_size = lax.axis_size("grp")
    node_dev = features.shape[0]
    tile_size = adjacency.shape[1]
    slots = adjacency.shape[0]
    width = features.shape[1]
    row_tiles = blk_size * node_dev // tile_size
    per_tile = tile_size // node_dev
    live = lax.iota(jnp.int32, slots) < count_here
    placing = (rows_here[:, None] == lax.iota(jnp.int32, row_tiles)[None, :]) & live[:, None]
    lhs = adjacency.transpose(1, 0, 2).reshape(tile_size, slots * tile_size)
    slot_mask = jnp.broadcast_to(placing.T[:, None, :, None], (row_tiles, 1, slots, tile_size))
    placed_lhs = jnp.where(
        slot_mask.reshape(row_tiles, 1, slots * tile_size), lhs[None], jnp.zeros((), lhs.dtype)
    ).reshape(row_tiles * tile_size, slots * tile_size)
    ones = jnp.ones((tile_size, 128), adjacency.dtype)
    slot_sums = jnp.einsum("tij,jk->tik", adjacency, ones, preferred_element_type=jnp.float32)[:, :, 0]
    degree_part = jnp.sum(
        jnp.where(placing.T[:, :, None], slot_sums[None], 0.0), axis=1
    ).reshape(blk_size, node_dev)
    degree = scatter_sum_pairs(degree_part, "blk", blk_size)
    scale = lax.rsqrt(1.0 + degree)[:, None]
    me_grp = lax.axis_index("grp")
    hidden = features
    result = None
    for layer_index in range(LAYERS):
        mixed = jnp.dot(hidden, weights[layer_index], preferred_element_type=jnp.float32)
        scaled = (mixed * scale).astype(jnp.bfloat16)
        if TWO_STAGE_GATHER and per_tile > 1 and grp_size % per_tile == 0:
            full = gather_outer_first(scaled, "grp", grp_size, per_tile, SPLIT)
            n_tiles = grp_size // per_tile
            ahead = (cols_here - me_grp // per_tile) % n_tiles
            from_pos = (lax.iota(jnp.int32, per_tile) - me_grp % per_tile) % per_tile
            blocks = full[from_pos[None, :], ahead[:, None]].reshape(slots, tile_size, width)
        else:
            received = gather_group(scaled, "grp", grp_size)
            sources = cols_here[:, None] * per_tile + lax.iota(jnp.int32, per_tile)[None, :]
            blocks = received[(sources - me_grp) % grp_size].reshape(slots, tile_size, width)
        out = jnp.dot(
            placed_lhs, blocks.reshape(slots * tile_size, width), preferred_element_type=jnp.float32
        )
        partial_value = out.reshape(blk_size, node_dev, width)
        summed = scatter_sum_pairs(partial_value, "blk", blk_size)
        pre = (summed + scaled.astype(jnp.float32)) * scale + biases[layer_index][None, :]
        if layer_index < LAYERS - 1:
            hidden = jnp.maximum(pre, 0.0).astype(jnp.bfloat16)
        else:
            result = pre.astype(jnp.bfloat16)
    return result


def solution(mesh):
    placed = (
        P(("blk", "grp"), None),
        P(),
        P(),
        P("blk", "grp", None, None, None),
        P("blk", "grp", None),
        P("blk", "grp", None),
        P("blk", "grp"),
    )
    return jax.shard_map(
        on_device, mesh=mesh, in_specs=placed, out_specs=P(("blk", "grp"), None), check_vma=False
    )
```
